256 devices in a mesh: sample: 16 (over x_hi, y, core), depth: 16 (over x_lo, z).
Axes of the slice: x: 4 (x_hi: 2, x_lo: 2; x = x_hi * 2 + x_lo), y: 4, z: 8, core: 2. Of those that a mesh axis runs over, the one named last changes fastest.
Arguments:
- layer_input: bfloat16 [16, 32, 32, 32, 128], P('sample', None, 'depth'), may hold values from -6 to 6
- preact: bfloat16 [16, 64, 32, 32, 128], P('sample', None, 'depth'), may hold values from -6 to 6
- cotangent: bfloat16 [16, 128, 16, 16, 64], P('sample', None, None, 'depth'), may hold values from -12 to 12
- kernel_mid: bfloat16 [27, 32, 64], replicated, may hold values from -0.21875 to 0.21875
- kernel_deep: bfloat16 [27, 64, 128], replicated, may hold values from -0.15625 to 0.15625
Outputs:
- grad_mid: float32 [27, 32, 64], replicated
- grad_deep: float32 [27, 64, 128], replicated
- data_grad: bfloat16 [16, 32, 32, 32, 128], P('sample', None, 'depth')
The draws below stay inside these ranges and needn't reach their ends.
All inputs are finite; a program needn't handle non-finite values.
Results may differ from the reference program's by a relative error of at most 0.007.
Values may be sent and summed in bfloat16 or wider, within the bound.
No kernel may reach another device: no remote copies, remote signals or barrier semaphores. Data moves between devices by JAX's collectives and lax.ppermute only.
A program may use at most 64 MiB of HBM per device.

```python
import math
import jax
import jax.numpy as jnp
from jax import lax

CIN = 32
CMID = 64
COUT = 128
HEIGHT = 32
WIDTH = 128
SAMPLES = 16
DEPTH = 32


def block_scale(stream_key, shape, cuts, smallest, largest):
    def one(position, parts):
        steps = jax.random.uniform(jax.random.fold_in(jax.random.fold_in(stream_key, 6), position), (parts,), jnp.float32, smallest / len(cuts), largest / len(cuts))
        return jnp.repeat(jnp.exp(steps), shape[position] // parts).reshape((-1,) + (1,) * (len(shape) - position - 1))

    gain = one(*cuts[0])
    for cut in cuts[1:]:
        gain = gain * one(*cut)
    return gain


def bell_draw(own_key, extent, spread, reach, split=(), held_as=jnp.bfloat16):
    drawn = jax.random.normal(own_key, extent, jnp.float32) * spread
    if len(split) > 0:
        drawn = block_scale(own_key, extent, split, -0.22, 0.18) * drawn
    return jnp.clip(drawn, min=-reach, max=reach).astype(held_as)


def setup_inputs(seed: int = 0) -> dict:
    key_of = jax.random.split(jax.random.key(seed), 6)
    layer_input = bell_draw(key_of[0], (SAMPLES, CIN, DEPTH, HEIGHT, WIDTH), 1.0, 6.0, ((0, 16), (2, 16)))
    preact = bell_draw(key_of[1], (SAMPLES, CMID, DEPTH, HEIGHT, WIDTH), 1.0, 6.0, ((0, 16), (2, 16)))
    cotangent = bell_draw(key_of[2], (SAMPLES, COUT, DEPTH // 2, HEIGHT // 2, WIDTH // 2), 2.0, 12.0, ((0, 16), (3, 16)))
    kernel_mid = bell_draw(key_of[3], (27, CIN, CMID), (27 * CIN) ** -0.5, 0.21875)
    kernel_deep = bell_draw(key_of[4], (27, CMID, COUT), (27 * CMID) ** -0.5, 0.15625)
    return {"layer_input": layer_input, "preact": preact, "cotangent": cotangent, "kernel_mid": kernel_mid, "kernel_deep": kernel_deep}


leak_slope = 0.3

def conv_back(inputs, cot_vol, kernel):
    slabs_n, rows_n, cols_n = (inputs.shape[1], inputs.shape[2], inputs.shape[3])
    widths = ((0, 0), (1, 1), (1, 1), (1, 1))
    in_padded = jnp.pad(inputs.astype(jnp.float32), widths)
    cot_f32 = cot_vol.astype(jnp.float32)
    cot_padded = jnp.pad(cot_f32, widths)
    kernel_f32 = kernel.astype(jnp.float32)
    pieces = []
    data_part = jnp.zeros((inputs.shape[0], slabs_n, rows_n, cols_n), jnp.float32)
    for along_z in range(3):
        for along_y in range(3):
            for along_x in range(3):
                offset = (along_z * 3 + along_y) * 3 + along_x
                shifted = in_padded[:, along_z:along_z + slabs_n, along_y:along_y + rows_n, along_x:along_x + cols_n]
                pieces.append(jnp.einsum('czhw,ozhw->co', shifted, cot_f32, precision=lax.Precision.HIGHEST))
                moved = cot_padded[:, 2 - along_z:2 - along_z + slabs_n, 2 - along_y:2 - along_y + rows_n, 2 - along_x:2 - along_x + cols_n]
                data_part = data_part + jnp.einsum('co,ozhw->czhw', kernel_f32[offset], moved, precision=lax.Precision.HIGHEST)
    return (jnp.stack(pieces), data_part)

def reference(layer_input, preact, cotangent, kernel_mid, kernel_deep):

    def one_sample(sample_items):
        input_vol, preact_vol, cot_vol = sample_items
        preact_f32 = preact_vol.astype(jnp.float32)
        activated = jnp.where(preact_f32 > 0, preact_f32, leak_slope * preact_f32)
        pooled = activated.reshape(CMID, DEPTH // 2, 2, HEIGHT // 2, 2, WIDTH // 2, 2).mean(axis=(2, 4, 6))
        pooled = lax.optimization_barrier(pooled.astype(jnp.bfloat16))
        deep_part, deep_data = conv_back(pooled, cot_vol, kernel_deep)
        deep_data = lax.optimization_barrier(deep_data.astype(jnp.bfloat16))
        expanded = jnp.broadcast_to(deep_data[:, :, None, :, None, :, None], (CMID, DEPTH // 2, 2, HEIGHT // 2, 2, WIDTH // 2, 2)).reshape(CMID, DEPTH, HEIGHT, WIDTH)
        mid_cot = expanded.astype(jnp.float32) * 0.125 * jnp.where(preact_f32 > 0, 1.0, leak_slope)
        mid_cot = lax.optimization_barrier(mid_cot.astype(jnp.bfloat16))
        mid_part, data_part = conv_back(input_vol, mid_cot, kernel_mid)
        return (mid_part, deep_part, data_part.astype(jnp.bfloat16))
    mid_parts, deep_parts, data_grads = lax.map(one_sample, (layer_input, preact, cotangent))
    cells = SAMPLES * DEPTH * HEIGHT * WIDTH
    grad_mid = lax.optimization_barrier(jnp.sum(mid_parts, axis=0)) * (1.0 / math.sqrt(cells))
    grad_deep = lax.optimization_barrier(jnp.sum(deep_parts, axis=0)) * (1.0 / math.sqrt(cells / 8))
    return (grad_mid, grad_deep, data_grads)
```

```python
import math

import jax
import jax.numpy as jnp
from jax import lax
from jax.sharding import PartitionSpec as P

leak_slope = 0.3


def padded(cells, sides, width):
    for axis, dim in sides:
        count = lax.axis_size(axis)
        ends = count - 1
        head = lax.slice_in_dim(cells, 0, width, axis=dim)
        tail = lax.slice_in_dim(cells, cells.shape[dim] - width, cells.shape[dim], axis=dim)
        cells = jnp.concatenate(
            [
                lax.ppermute(tail, axis, [(i, (i + 1) % count) for i in range(ends)]),
                cells,
                lax.ppermute(head, axis, [((i + 1) % count, i) for i in range(ends)]),
            ],
            axis=dim,
        )
    return cells


def pad_spatial(volume, halo_dim):
    widths = [(0, 0), (1, 1), (1, 1), (1, 1)]
    widths[halo_dim] = (0, 0)
    return jnp.pad(volume, widths)


def local_back(in_padded, cot_padded, kernel, slabs_n, rows_n, cols_n):
    center = cot_padded[:, 1 : 1 + slabs_n, 1 : 1 + rows_n, 1 : 1 + cols_n]
    data_part = jnp.zeros((in_padded.shape[0], slabs_n, rows_n, cols_n), jnp.float32)
    pieces = []
    for along_z in range(3):
        for along_y in range(3):
            for along_x in range(3):
                offset = (along_z * 3 + along_y) * 3 + along_x
                shifted = in_padded[
                    :,
                    along_z : along_z + slabs_n,
                    along_y : along_y + rows_n,
                    along_x : along_x + cols_n,
                ]
                pieces.append(
                    jnp.einsum("czhw,ozhw->co", shifted, center, preferred_element_type=jnp.float32)
                )
                moved = cot_padded[
                    :,
                    2 - along_z : 2 - along_z + slabs_n,
                    2 - along_y : 2 - along_y + rows_n,
                    2 - along_x : 2 - along_x + cols_n,
                ]
                data_part = data_part + jnp.einsum(
                    "co,ozhw->czhw", kernel[offset], moved, preferred_element_type=jnp.float32
                )
    return (jnp.stack(pieces), data_part)


def summed_everywhere(parts):
    flat = jnp.concatenate([p.reshape(-1) for p in parts])
    depth_n = lax.axis_size("depth")
    sample_n = lax.axis_size("sample")
    total = flat.shape[0]
    per_depth = total // depth_n
    per_all = per_depth // sample_n
    step = lax.all_to_all(flat.reshape(depth_n, per_depth), "depth", 0, 0, tiled=True).sum(0)
    step = lax.all_to_all(step.reshape(sample_n, per_all), "sample", 0, 0, tiled=True).sum(0)
    step = lax.all_to_all(jnp.broadcast_to(step[None], (sample_n, per_all)), "sample", 0, 0, tiled=True)
    step = lax.all_to_all(
        jnp.broadcast_to(step.reshape(1, per_depth), (depth_n, per_depth)), "depth", 0, 0, tiled=True
    ).reshape(total)
    out = []
    start = 0
    for p in parts:
        out.append(step[start : start + p.size].reshape(p.shape))
        start += p.size
    return tuple(out)


def body(layer_input, preact, cotangent, kernel_mid, kernel_deep):
    input_slab = layer_input[0]
    preact_slab = preact[0]
    deep_cot = cotangent[0]
    chan_mid, slabs_n, rows_n, cols_n = preact_slab.shape
    input_halo = padded(input_slab, (("depth", 1),), 1)
    input_padded = pad_spatial(input_halo, 1)
    preact_f32 = preact_slab.astype(jnp.float32)
    activated = jnp.where(preact_f32 > 0, preact_f32, leak_slope * preact_f32)
    pooled = (
        activated.reshape(chan_mid, slabs_n // 2, 2, rows_n // 2, 2, cols_n // 2, 2)
        .mean(axis=(2, 4, 6))
        .astype(jnp.bfloat16)
    )
    slab_cot = lax.all_to_all(deep_cot, "depth", split_axis=1, concat_axis=2, tiled=True)
    joined = jnp.concatenate([pooled, slab_cot], axis=0)
    joined_halo = padded(joined, (("depth", 1),), 1)
    joined_pad = pad_spatial(joined_halo, 1)
    deep_part, deep_data = local_back(
        joined_pad[:chan_mid],
        joined_pad[chan_mid:],
        kernel_deep,
        slabs_n // 2,
        rows_n // 2,
        cols_n // 2,
    )
    deep_data = deep_data.astype(jnp.bfloat16)
    expanded = jnp.broadcast_to(
        deep_data[:, :, None, :, None, :, None],
        (chan_mid, slabs_n // 2, 2, rows_n // 2, 2, cols_n // 2, 2),
    ).reshape(chan_mid, slabs_n, rows_n, cols_n)
    mid_cot = (
        expanded.astype(jnp.float32) * 0.125 * jnp.where(preact_f32 > 0, 1.0, leak_slope)
    ).astype(jnp.bfloat16)
    cot_halo = padded(mid_cot, (("depth", 1),), 1)
    mid_part, data_part = local_back(
        input_padded, pad_spatial(cot_halo, 1), kernel_mid, slabs_n, rows_n, cols_n
    )
    deep_sum, mid_sum = summed_everywhere((deep_part, mid_part))
    cells = lax.axis_size("sample") * lax.axis_size("depth") * slabs_n * rows_n * cols_n
    grad_mid = mid_sum * (1.0 / math.sqrt(cells))
    grad_deep = deep_sum * (1.0 / math.sqrt(cells / 8))
    return (grad_mid, grad_deep, data_part.astype(jnp.bfloat16)[None])


def solution(mesh):
    return jax.shard_map(
        body,
        mesh=mesh,
        in_specs=(
            P("sample", None, "depth", None, None),
            P("sample", None, "depth", None, None),
            P("sample", None, None, "depth", None),
            P(),
            P(),
        ),
        out_specs=(P(), P(), P("sample", None, "depth", None, None)),
        check_vma=False,
    )
```

```python
import math

import jax
import jax.numpy as jnp
from jax import lax
from jax.sharding import PartitionSpec as P

leak_slope = 0.3


def padded(cells, sides, width):
    for axis, dim in sides:
        count = lax.axis_size(axis)
        ends = count - 1
        head = lax.slice_in_dim(cells, 0, width, axis=dim)
        tail = lax.slice_in_dim(cells, cells.shape[dim] - width, cells.shape[dim], axis=dim)
        cells = jnp.concatenate(
            [
                lax.ppermute(tail, axis, [(i, (i + 1) % count) for i in range(ends)]),
                cells,
                lax.ppermute(head, axis, [((i + 1) % count, i) for i in range(ends)]),
            ],
            axis=dim,
        )
    return cells


def pad_spatial(volume, halo_dim):
    widths = [(0, 0), (1, 1), (1, 1), (1, 1)]
    widths[halo_dim] = (0, 0)
    return jnp.pad(volume, widths)


def local_back(in_padded, cot_padded, kernel, slabs_n, rows_n, cols_n):
    chans = in_padded.shape[0]
    outs = cot_padded.shape[0]
    center = cot_padded[:, 1 : 1 + slabs_n, 1 : 1 + rows_n, 1 : 1 + cols_n]
    taps = lax.conv_general_dilated(
        in_padded[:, None],
        center[:, None],
        (1, 1, 1),
        "VALID",
        dimension_numbers=("NCDHW", "OIDHW", "NCDHW"),
        preferred_element_type=jnp.float32,
    )
    pieces = taps.transpose(2, 3, 4, 0, 1).reshape(27, chans, outs)
    flipped = kernel.reshape(3, 3, 3, chans, outs)[::-1, ::-1, ::-1].transpose(3, 4, 0, 1, 2)
    data_part = lax.conv_general_dilated(
        cot_padded[None],
        flipped,
        (1, 1, 1),
        "VALID",
        dimension_numbers=("NCDHW", "OIDHW", "NCDHW"),
        preferred_element_type=jnp.float32,
    )[0]
    return (pieces, data_part)


def summed_everywhere(parts):
    flat = jnp.concatenate([p.reshape(-1) for p in parts])
    depth_n = lax.axis_size("depth")
    sample_n = lax.axis_size("sample")
    total = flat.shape[0]
    per_depth = total // depth_n
    per_all = per_depth // sample_n
    step = lax.all_to_all(flat.reshape(depth_n, per_depth), "depth", 0, 0, tiled=True).sum(0)
    step = lax.all_to_all(step.reshape(sample_n, per_all), "sample", 0, 0, tiled=True).sum(0)
    step = lax.all_to_all(jnp.broadcast_to(step[None], (sample_n, per_all)), "sample", 0, 0, tiled=True)
    step = lax.all_to_all(
        jnp.broadcast_to(step.reshape(1, per_depth), (depth_n, per_depth)), "depth", 0, 0, tiled=True
    ).reshape(total)
    out = []
    start = 0
    for p in parts:
        out.append(step[start : start + p.size].reshape(p.shape))
        start += p.size
    return tuple(out)


def body(layer_input, preact, cotangent, kernel_mid, kernel_deep):
    input_slab = layer_input[0]
    preact_slab = preact[0]
    deep_cot = cotangent[0]
    chan_mid, slabs_n, rows_n, cols_n = preact_slab.shape
    input_halo = padded(input_slab, (("depth", 1),), 1)
    input_padded = pad_spatial(input_halo, 1)
    preact_f32 = preact_slab.astype(jnp.float32)
    activated = jnp.where(preact_f32 > 0, preact_f32, leak_slope * preact_f32)
    pooled = (
        activated.reshape(chan_mid, slabs_n // 2, 2, rows_n // 2, 2, cols_n // 2, 2)
        .mean(axis=(2, 4, 6))
        .astype(jnp.bfloat16)
    )
    slab_cot = lax.all_to_all(deep_cot, "depth", split_axis=1, concat_axis=2, tiled=True)
    joined = jnp.concatenate([pooled, slab_cot], axis=0)
    joined_halo = padded(joined, (("depth", 1),), 1)
    joined_pad = pad_spatial(joined_halo, 1)
    deep_part, deep_data = local_back(
        joined_pad[:chan_mid],
        joined_pad[chan_mid:],
        kernel_deep,
        slabs_n // 2,
        rows_n // 2,
        cols_n // 2,
    )
    deep_data = deep_data.astype(jnp.bfloat16)
    expanded = jnp.broadcast_to(
        deep_data[:, :, None, :, None, :, None],
        (chan_mid, slabs_n // 2, 2, rows_n // 2, 2, cols_n // 2, 2),
    ).reshape(chan_mid, slabs_n, rows_n, cols_n)
    mid_cot = (
        expanded.astype(jnp.float32) * 0.125 * jnp.where(preact_f32 > 0, 1.0, leak_slope)
    ).astype(jnp.bfloat16)
    cot_halo = padded(mid_cot, (("depth", 1),), 1)
    mid_part, data_part = local_back(
        input_padded, pad_spatial(cot_halo, 1), kernel_mid, slabs_n, rows_n, cols_n
    )
    deep_sum, mid_sum = summed_everywhere((deep_part, mid_part))
    cells = lax.axis_size("sample") * lax.axis_size("depth") * slabs_n * rows_n * cols_n
    grad_mid = mid_sum * (1.0 / math.sqrt(cells))
    grad_deep = deep_sum * (1.0 / math.sqrt(cells / 8))
    return (grad_mid, grad_deep, data_part.astype(jnp.bfloat16)[None])


def solution(mesh):
    return jax.shard_map(
        body,
        mesh=mesh,
        in_specs=(
            P("sample", None, "depth", None, None),
            P("sample", None, "depth", None, None),
            P("sample", None, None, "depth", None),
            P(),
            P(),
        ),
        out_specs=(P(), P(), P("sample", None, "depth", None, None)),
        check_vma=False,
    )
```

```python
import math

import jax
import jax.numpy as jnp
from jax import lax
from jax.sharding import PartitionSpec as P

leak_slope = 0.3


def padded(cells, sides, width):
    for axis, dim in sides:
        count = lax.axis_size(axis)
        ends = count - 1
        head = lax.slice_in_dim(cells, 0, width, axis=dim)
        tail = lax.slice_in_dim(cells, cells.shape[dim] - width, cells.shape[dim], axis=dim)
        cells = jnp.concatenate(
            [
                lax.ppermute(tail, axis, [(i, (i + 1) % count) for i in range(ends)]),
                cells,
                lax.ppermute(head, axis, [((i + 1) % count, i) for i in range(ends)]),
            ],
            axis=dim,
        )
    return cells


def pad_spatial(volume, halo_dim):
    widths = [(0, 0), (1, 1), (1, 1), (1, 1)]
    widths[halo_dim] = (0, 0)
    return jnp.pad(volume, widths)


def local_back(in_padded, cot_padded, kernel, slabs_n, rows_n, cols_n):
    center = cot_padded[:, 1 : 1 + slabs_n, 1 : 1 + rows_n, 1 : 1 + cols_n]
    data_part = jnp.zeros((in_padded.shape[0], slabs_n, rows_n, cols_n), jnp.float32)
    pieces = []
    for along_z in range(3):
        for along_y in range(3):
            for along_x in range(3):
                offset = (along_z * 3 + along_y) * 3 + along_x
                shifted = in_padded[
                    :,
                    along_z : along_z + slabs_n,
                    along_y : along_y + rows_n,
                    along_x : along_x + cols_n,
                ]
                pieces.append(
                    jnp.einsum("czhw,ozhw->co", shifted, center, preferred_element_type=jnp.float32)
                )
                moved = cot_padded[
                    :,
                    2 - along_z : 2 - along_z + slabs_n,
                    2 - along_y : 2 - along_y + rows_n,
                    2 - along_x : 2 - along_x + cols_n,
                ]
                data_part = data_part + jnp.einsum(
                    "co,ozhw->czhw", kernel[offset], moved, preferred_element_type=jnp.float32
                )
    return (jnp.stack(pieces), data_part)


def summed_everywhere(parts):
    flat = jnp.concatenate([p.reshape(-1) for p in parts])
    depth_n = lax.axis_size("depth")
    sample_n = lax.axis_size("sample")
    total = flat.shape[0]
    per_depth = total // depth_n
    per_all = per_depth // sample_n
    step = lax.all_to_all(flat.reshape(depth_n, per_depth), "depth", 0, 0, tiled=True).sum(0)
    step = lax.all_to_all(step.reshape(sample_n, per_all), "sample", 0, 0, tiled=True).sum(0)
    step = lax.all_to_all(jnp.broadcast_to(step[None], (sample_n, per_all)), "sample", 0, 0, tiled=True)
    step = lax.all_to_all(
        jnp.broadcast_to(step.reshape(1, per_depth), (depth_n, per_depth)), "depth", 0, 0, tiled=True
    ).reshape(total)
    out = []
    start = 0
    for p in parts:
        out.append(step[start : start + p.size].reshape(p.shape))
        start += p.size
    return tuple(out)


def body(layer_input, preact, cotangent, kernel_mid, kernel_deep):
    input_slab = layer_input[0]
    preact_slab = preact[0]
    deep_cot = cotangent[0]
    chan_mid, slabs_n, rows_n, cols_n = preact_slab.shape
    input_halo = padded(input_slab, (("depth", 1),), 1)
    input_padded = pad_spatial(input_halo, 1)
    preact_f32 = preact_slab.astype(jnp.float32)
    activated = jnp.where(preact_f32 > 0, preact_f32, leak_slope * preact_f32)
    pooled = (
        activated.reshape(chan_mid, slabs_n // 2, 2, rows_n // 2, 2, cols_n // 2, 2)
        .mean(axis=(2, 4, 6))
        .astype(jnp.bfloat16)
    )
    slab_cot = lax.all_to_all(deep_cot, "depth", split_axis=1, concat_axis=2, tiled=True)
    joined = jnp.concatenate([pooled, slab_cot], axis=0)
    joined_halo = padded(joined, (("depth", 1),), 1)
    joined_pad = pad_spatial(joined_halo, 1)
    deep_part, deep_data = local_back(
        joined_pad[:chan_mid],
        joined_pad[chan_mid:],
        kernel_deep,
        slabs_n // 2,
        rows_n // 2,
        cols_n // 2,
    )
    (deep_sum,) = summed_everywhere((deep_part,))
    deep_data = deep_data.astype(jnp.bfloat16)
    expanded = jnp.broadcast_to(
        deep_data[:, :, None, :, None, :, None],
        (chan_mid, slabs_n // 2, 2, rows_n // 2, 2, cols_n // 2, 2),
    ).reshape(chan_mid, slabs_n, rows_n, cols_n)
    mid_cot = (
        expanded.astype(jnp.float32) * 0.125 * jnp.where(preact_f32 > 0, 1.0, leak_slope)
    ).astype(jnp.bfloat16)
    cot_halo = padded(mid_cot, (("depth", 1),), 1)
    mid_part, data_part = local_back(
        input_padded, pad_spatial(cot_halo, 1), kernel_mid, slabs_n, rows_n, cols_n
    )
    (mid_sum,) = summed_everywhere((mid_part,))
    cells = lax.axis_size("sample") * lax.axis_size("depth") * slabs_n * rows_n * cols_n
    grad_mid = mid_sum * (1.0 / math.sqrt(cells))
    grad_deep = deep_sum * (1.0 / math.sqrt(cells / 8))
    return (grad_mid, grad_deep, data_part.astype(jnp.bfloat16)[None])


def solution(mesh):
    return jax.shard_map(
        body,
        mesh=mesh,
        in_specs=(
            P("sample", None, "depth", None, None),
            P("sample", None, "depth", None, None),
            P("sample", None, None, "depth", None),
            P(),
            P(),
        ),
        out_specs=(P(), P(), P("sample", None, "depth", None, None)),
        check_vma=False,
    )
```

```python
import math

import jax
import jax.numpy as jnp
from jax import lax
from jax.sharding import PartitionSpec as P

leak_slope = 0.3


def padded(cells, sides, width):
    for axis, dim in sides:
        count = lax.axis_size(axis)
        ends = count - 1
        head = lax.slice_in_dim(cells, 0, width, axis=dim)
        tail = lax.slice_in_dim(cells, cells.shape[dim] - width, cells.shape[dim], axis=dim)
        cells = jnp.concatenate(
            [
                lax.ppermute(tail, axis, [(i, (i + 1) % count) for i in range(ends)]),
                cells,
                lax.ppermute(head, axis, [((i + 1) % count, i) for i in range(ends)]),
            ],
            axis=dim,
        )
    return cells


def pad_spatial(volume, halo_dim):
    widths = [(0, 0), (1, 1), (1, 1), (1, 1)]
    widths[halo_dim] = (0, 0)
    return jnp.pad(volume, widths)


def local_back(in_padded, cot_padded, kernel, slabs_n, rows_n, cols_n):
    center = cot_padded[:, 1 : 1 + slabs_n, 1 : 1 + rows_n, 1 : 1 + cols_n]
    data_part = jnp.zeros((in_padded.shape[0], slabs_n, rows_n, cols_n), jnp.float32)
    pieces = []
    for along_z in range(3):
        for along_y in range(3):
            for along_x in range(3):
                offset = (along_z * 3 + along_y) * 3 + along_x
                shifted = in_padded[
                    :,
                    along_z : along_z + slabs_n,
                    along_y : along_y + rows_n,
                    along_x : along_x + cols_n,
                ]
                pieces.append(
                    jnp.einsum("czhw,ozhw->co", shifted, center, preferred_element_type=jnp.float32)
                )
                moved = cot_padded[
                    :,
                    2 - along_z : 2 - along_z + slabs_n,
                    2 - along_y : 2 - along_y + rows_n,
                    2 - along_x : 2 - along_x + cols_n,
                ]
                data_part = data_part + jnp.einsum(
                    "co,ozhw->czhw", kernel[offset], moved, preferred_element_type=jnp.float32
                )
    return (jnp.stack(pieces), data_part)


def summed_everywhere(parts):
    flat = jnp.concatenate([p.reshape(-1) for p in parts])
    depth_n = lax.axis_size("depth")
    sample_n = lax.axis_size("sample")
    total = flat.shape[0]
    per_depth = total // depth_n
    per_all = per_depth // sample_n
    step = lax.all_to_all(flat.reshape(depth_n, per_depth), "depth", 0, 0, tiled=True).sum(0)
    step = lax.all_to_all(step.reshape(sample_n, per_all), "sample", 0, 0, tiled=True).sum(0)
    step = lax.all_to_all(jnp.broadcast_to(step[None], (sample_n, per_all)), "sample", 0, 0, tiled=True)
    step = lax.all_to_all(
        jnp.broadcast_to(step.reshape(1, per_depth), (depth_n, per_depth)), "depth", 0, 0, tiled=True
    ).reshape(total)
    out = []
    start = 0
    for p in parts:
        out.append(step[start : start + p.size].reshape(p.shape))
        start += p.size
    return tuple(out)


def tap_shift(cells, along_z, along_y, along_x, slabs_n, rows_n, cols_n):
    return cells[
        :,
        along_z : along_z + slabs_n,
        along_y : along_y + rows_n,
        along_x : along_x + cols_n,
    ]


def mid_back(in_padded, cot_padded, kernel, deep_part, slabs_n, rows_n, cols_n):
    center = cot_padded[:, 1 : 1 + slabs_n, 1 : 1 + rows_n, 1 : 1 + cols_n]
    taps = [(z, y, x) for z in range(3) for y in range(3) for x in range(3)]
    pieces = [
        jnp.einsum(
            "czhw,ozhw->co",
            tap_shift(in_padded, z, y, x, slabs_n, rows_n, cols_n),
            center,
            preferred_element_type=jnp.float32,
        )
        for z, y, x in taps
    ]
    mid_part = jnp.stack(pieces)

    def add_taps(data_part, cot_now, chosen):
        for z, y, x in chosen:
            moved = tap_shift(cot_now, 2 - z, 2 - y, 2 - x, slabs_n, rows_n, cols_n)
            data_part = data_part + jnp.einsum(
                "co,ozhw->czhw", kernel[(z * 3 + y) * 3 + x], moved, preferred_element_type=jnp.float32
            )
        return data_part

    parts = (deep_part, mid_part)
    flat = jnp.concatenate([p.reshape(-1) for p in parts])
    depth_n = lax.axis_size("depth")
    sample_n = lax.axis_size("sample")
    total = flat.shape[0]
    per_depth = total // depth_n
    per_all = per_depth // sample_n
    data_part = jnp.zeros((in_padded.shape[0], slabs_n, rows_n, cols_n), jnp.float32)
    step = lax.all_to_all(flat.reshape(depth_n, per_depth), "depth", 0, 0, tiled=True)
    data_part = add_taps(data_part, cot_padded, taps[0:7])
    step, data_part, cot_now = lax.optimization_barrier((step, data_part, cot_padded))
    step = lax.all_to_all(step.sum(0).reshape(sample_n, per_all), "sample", 0, 0, tiled=True)
    data_part = add_taps(data_part, cot_now, taps[7:14])
    step, data_part, cot_now = lax.optimization_barrier((step, data_part, cot_padded))
    step = lax.all_to_all(jnp.broadcast_to(step.sum(0)[None], (sample_n, per_all)), "sample", 0, 0, tiled=True)
    data_part = add_taps(data_part, cot_now, taps[14:21])
    step, data_part, cot_now = lax.optimization_barrier((step, data_part, cot_padded))
    step = lax.all_to_all(
        jnp.broadcast_to(step.reshape(1, per_depth), (depth_n, per_depth)), "depth", 0, 0, tiled=True
    ).reshape(total)
    data_part = add_taps(data_part, cot_now, taps[21:27])
    sums = []
    start = 0
    for p in parts:
        sums.append(step[start : start + p.size].reshape(p.shape))
        start += p.size
    return sums[0], sums[1], data_part


def body(layer_input, preact, cotangent, kernel_mid, kernel_deep):
    input_slab = layer_input[0]
    preact_slab = preact[0]
    deep_cot = cotangent[0]
    chan_mid, slabs_n, rows_n, cols_n = preact_slab.shape
    input_halo = padded(input_slab, (("depth", 1),), 1)
    input_padded = pad_spatial(input_halo, 1)
    preact_f32 = preact_slab.astype(jnp.float32)
    activated = jnp.where(preact_f32 > 0, preact_f32, leak_slope * preact_f32)
    pooled = (
        activated.reshape(chan_mid, slabs_n // 2, 2, rows_n // 2, 2, cols_n // 2, 2)
        .mean(axis=(2, 4, 6))
        .astype(jnp.bfloat16)
    )
    slab_cot = lax.all_to_all(deep_cot, "depth", split_axis=1, concat_axis=2, tiled=True)
    joined = jnp.concatenate([pooled, slab_cot], axis=0)
    joined_halo = padded(joined, (("depth", 1),), 1)
    joined_pad = pad_spatial(joined_halo, 1)
    deep_part, deep_data = local_back(
        joined_pad[:chan_mid],
        joined_pad[chan_mid:],
        kernel_deep,
        slabs_n // 2,
        rows_n // 2,
        cols_n // 2,
    )
    deep_data = deep_data.astype(jnp.bfloat16)
    expanded = jnp.broadcast_to(
        deep_data[:, :, None, :, None, :, None],
        (chan_mid, slabs_n // 2, 2, rows_n // 2, 2, cols_n // 2, 2),
    ).reshape(chan_mid, slabs_n, rows_n, cols_n)
    mid_cot = (
        expanded.astype(jnp.float32) * 0.125 * jnp.where(preact_f32 > 0, 1.0, leak_slope)
    ).astype(jnp.bfloat16)
    cot_halo = padded(mid_cot, (("depth", 1),), 1)
    deep_sum, mid_sum, data_part = mid_back(
        input_padded, pad_spatial(cot_halo, 1), kernel_mid, deep_part, slabs_n, rows_n, cols_n
    )
    cells = lax.axis_size("sample") * lax.axis_size("depth") * slabs_n * rows_n * cols_n
    grad_mid = mid_sum * (1.0 / math.sqrt(cells))
    grad_deep = deep_sum * (1.0 / math.sqrt(cells / 8))
    return (grad_mid, grad_deep, data_part.astype(jnp.bfloat16)[None])


def solution(mesh):
    return jax.shard_map(
        body,
        mesh=mesh,
        in_specs=(
            P("sample", None, "depth", None, None),
            P("sample", None, "depth", None, None),
            P("sample", None, None, "depth", None),
            P(),
            P(),
        ),
        out_specs=(P(), P(), P("sample", None, "depth", None, None)),
        check_vma=False,
    )
```

```python
import math

import jax
import jax.numpy as jnp
from jax import lax
from jax.sharding import PartitionSpec as P

leak_slope = 0.3


def padded(cells, sides, width):
    for axis, dim in sides:
        count = lax.axis_size(axis)
        ends = count - 1
        head = lax.slice_in_dim(cells, 0, width, axis=dim)
        tail = lax.slice_in_dim(cells, cells.shape[dim] - width, cells.shape[dim], axis=dim)
        cells = jnp.concatenate(
            [
                lax.ppermute(tail, axis, [(i, (i + 1) % count) for i in range(ends)]),
                cells,
                lax.ppermute(head, axis, [((i + 1) % count, i) for i in range(ends)]),
            ],
            axis=dim,
        )
    return cells


def pad_spatial(volume, halo_dim):
    widths = [(0, 0), (1, 1), (1, 1), (1, 1)]
    widths[halo_dim] = (0, 0)
    return jnp.pad(volume, widths)


def local_back(in_padded, cot_padded, kernel, slabs_n, rows_n, cols_n):
    center = cot_padded[:, 1 : 1 + slabs_n, 1 : 1 + rows_n, 1 : 1 + cols_n]
    data_part = jnp.zeros((in_padded.shape[0], slabs_n, rows_n, cols_n), jnp.float32)
    pieces = []
    for along_z in range(3):
        for along_y in range(3):
            for along_x in range(3):
                offset = (along_z * 3 + along_y) * 3 + along_x
                shifted = in_padded[
                    :,
                    along_z : along_z + slabs_n,
                    along_y : along_y + rows_n,
                    along_x : along_x + cols_n,
                ]
                pieces.append(
                    jnp.einsum("czhw,ozhw->co", shifted, center, preferred_element_type=jnp.float32)
                )
                moved = cot_padded[
                    :,
                    2 - along_z : 2 - along_z + slabs_n,
                    2 - along_y : 2 - along_y + rows_n,
                    2 - along_x : 2 - along_x + cols_n,
                ]
                data_part = data_part + jnp.einsum(
                    "co,ozhw->czhw", kernel[offset], moved, preferred_element_type=jnp.float32
                )
    return (jnp.stack(pieces), data_part)


def summed_everywhere(parts):
    flat = jnp.concatenate([p.reshape(-1) for p in parts])
    depth_n = lax.axis_size("depth")
    sample_n = lax.axis_size("sample")
    total = flat.shape[0]
    per_depth = total // depth_n
    per_all = per_depth // sample_n
    step = lax.all_to_all(flat.reshape(depth_n, per_depth), "depth", 0, 0, tiled=True).sum(0)
    step = lax.all_to_all(step.reshape(sample_n, per_all), "sample", 0, 0, tiled=True).sum(0)
    step = lax.all_to_all(jnp.broadcast_to(step[None], (sample_n, per_all)), "sample", 0, 0, tiled=True)
    step = lax.all_to_all(
        jnp.broadcast_to(step.reshape(1, per_depth), (depth_n, per_depth)), "depth", 0, 0, tiled=True
    ).reshape(total)
    out = []
    start = 0
    for p in parts:
        out.append(step[start : start + p.size].reshape(p.shape))
        start += p.size
    return tuple(out)


def tap_shift(cells, along_z, along_y, along_x, slabs_n, rows_n, cols_n):
    return cells[
        :,
        along_z : along_z + slabs_n,
        along_y : along_y + rows_n,
        along_x : along_x + cols_n,
    ]


def mid_back(in_padded, cot_padded, kernel, deep_part, slabs_n, rows_n, cols_n):
    center = cot_padded[:, 1 : 1 + slabs_n, 1 : 1 + rows_n, 1 : 1 + cols_n]
    taps = [(z, y, x) for z in range(3) for y in range(3) for x in range(3)]
    pieces = [
        jnp.einsum(
            "czhw,ozhw->co",
            tap_shift(in_padded, z, y, x, slabs_n, rows_n, cols_n),
            center,
            preferred_element_type=jnp.float32,
        )
        for z, y, x in taps
    ]
    mid_part = jnp.stack(pieces)

    def add_taps(data_part, cot_now, chosen):
        for z, y, x in chosen:
            moved = tap_shift(cot_now, 2 - z, 2 - y, 2 - x, slabs_n, rows_n, cols_n)
            data_part = data_part + jnp.einsum(
                "co,ozhw->czhw", kernel[(z * 3 + y) * 3 + x], moved, preferred_element_type=jnp.float32
            )
        return data_part

    parts = (deep_part, mid_part)
    flat = jnp.concatenate([p.reshape(-1) for p in parts])
    first_n = lax.axis_size("sample")
    second_n = lax.axis_size("depth")
    total = flat.shape[0]
    per_first = total // first_n
    per_all = per_first // second_n
    data_part = jnp.zeros((in_padded.shape[0], slabs_n, rows_n, cols_n), jnp.float32)
    step = lax.all_to_all(flat.reshape(first_n, per_first), "sample", 0, 0, tiled=True)
    data_part = add_taps(data_part, cot_padded, taps[0:7])
    step, data_part, cot_now = lax.optimization_barrier((step, data_part, cot_padded))
    step = lax.all_to_all(step.sum(0).reshape(second_n, per_all), "depth", 0, 0, tiled=True)
    data_part = add_taps(data_part, cot_now, taps[7:14])
    step, data_part, cot_now = lax.optimization_barrier((step, data_part, cot_padded))
    step = lax.all_to_all(jnp.broadcast_to(step.sum(0)[None], (second_n, per_all)), "depth", 0, 0, tiled=True)
    data_part = add_taps(data_part, cot_now, taps[14:21])
    step, data_part, cot_now = lax.optimization_barrier((step, data_part, cot_padded))
    step = lax.all_to_all(
        jnp.broadcast_to(step.reshape(1, per_first), (first_n, per_first)), "sample", 0, 0, tiled=True
    ).reshape(total)
    data_part = add_taps(data_part, cot_now, taps[21:27])
    sums = []
    start = 0
    for p in parts:
        sums.append(step[start : start + p.size].reshape(p.shape))
        start += p.size
    return sums[0], sums[1], data_part


def body(layer_input, preact, cotangent, kernel_mid, kernel_deep):
    input_slab = layer_input[0]
    preact_slab = preact[0]
    deep_cot = cotangent[0]
    chan_mid, slabs_n, rows_n, cols_n = preact_slab.shape
    input_halo = padded(input_slab, (("depth", 1),), 1)
    input_padded = pad_spatial(input_halo, 1)
    preact_f32 = preact_slab.astype(jnp.float32)
    activated = jnp.where(preact_f32 > 0, preact_f32, leak_slope * preact_f32)
    pooled = (
        activated.reshape(chan_mid, slabs_n // 2, 2, rows_n // 2, 2, cols_n // 2, 2)
        .mean(axis=(2, 4, 6))
        .astype(jnp.bfloat16)
    )
    slab_cot = lax.all_to_all(deep_cot, "depth", split_axis=1, concat_axis=2, tiled=True)
    joined = jnp.concatenate([pooled, slab_cot], axis=0)
    joined_halo = padded(joined, (("depth", 1),), 1)
    joined_pad = pad_spatial(joined_halo, 1)
    deep_part, deep_data = local_back(
        joined_pad[:chan_mid],
        joined_pad[chan_mid:],
        kernel_deep,
        slabs_n // 2,
        rows_n // 2,
        cols_n // 2,
    )
    deep_data = deep_data.astype(jnp.bfloat16)
    expanded = jnp.broadcast_to(
        deep_data[:, :, None, :, None, :, None],
        (chan_mid, slabs_n // 2, 2, rows_n // 2, 2, cols_n // 2, 2),
    ).reshape(chan_mid, slabs_n, rows_n, cols_n)
    mid_cot = (
        expanded.astype(jnp.float32) * 0.125 * jnp.where(preact_f32 > 0, 1.0, leak_slope)
    ).astype(jnp.bfloat16)
    cot_halo = padded(mid_cot, (("depth", 1),), 1)
    deep_sum, mid_sum, data_part = mid_back(
        input_padded, pad_spatial(cot_halo, 1), kernel_mid, deep_part, slabs_n, rows_n, cols_n
    )
    cells = lax.axis_size("sample") * lax.axis_size("depth") * slabs_n * rows_n * cols_n
    grad_mid = mid_sum * (1.0 / math.sqrt(cells))
    grad_deep = deep_sum * (1.0 / math.sqrt(cells / 8))
    return (grad_mid, grad_deep, data_part.astype(jnp.bfloat16)[None])


def solution(mesh):
    return jax.shard_map(
        body,
        mesh=mesh,
        in_specs=(
            P("sample", None, "depth", None, None),
            P("sample", None, "depth", None, None),
            P("sample", None, None, "depth", None),
            P(),
            P(),
        ),
        out_specs=(P(), P(), P("sample", None, "depth", None, None)),
        check_vma=False,
    )
```

```python
import math

import jax
import jax.numpy as jnp
from jax import lax
from jax.sharding import PartitionSpec as P

leak_slope = 0.3


def padded(cells, sides, width):
    for axis, dim in sides:
        count = lax.axis_size(axis)
        ends = count - 1
        head = lax.slice_in_dim(cells, 0, width, axis=dim)
        tail = lax.slice_in_dim(cells, cells.shape[dim] - width, cells.shape[dim], axis=dim)
        cells = jnp.concatenate(
            [
                lax.ppermute(tail, axis, [(i, (i + 1) % count) for i in range(ends)]),
                cells,
                lax.ppermute(head, axis, [((i + 1) % count, i) for i in range(ends)]),
            ],
            axis=dim,
        )
    return cells


def pad_spatial(volume, halo_dim):
    widths = [(0, 0), (1, 1), (1, 1), (1, 1)]
    widths[halo_dim] = (0, 0)
    return jnp.pad(volume, widths)


def local_back(in_padded, cot_padded, kernel, slabs_n, rows_n, cols_n):
    center = cot_padded[:, 1 : 1 + slabs_n, 1 : 1 + rows_n, 1 : 1 + cols_n]
    data_part = jnp.zeros((in_padded.shape[0], slabs_n, rows_n, cols_n), jnp.float32)
    pieces = []
    for along_z in range(3):
        for along_y in range(3):
            for along_x in range(3):
                offset = (along_z * 3 + along_y) * 3 + along_x
                shifted = in_padded[
                    :,
                    along_z : along_z + slabs_n,
                    along_y : along_y + rows_n,
                    along_x : along_x + cols_n,
                ]
                pieces.append(
                    jnp.einsum("czhw,ozhw->co", shifted, center, preferred_element_type=jnp.float32)
                )
                moved = cot_padded[
                    :,
                    2 - along_z : 2 - along_z + slabs_n,
                    2 - along_y : 2 - along_y + rows_n,
                    2 - along_x : 2 - along_x + cols_n,
                ]
                data_part = data_part + jnp.einsum(
                    "co,ozhw->czhw", kernel[offset], moved, preferred_element_type=jnp.float32
                )
    return (jnp.stack(pieces), data_part)


def summed_everywhere(parts):
    flat = jnp.concatenate([p.reshape(-1) for p in parts])
    depth_n = lax.axis_size("depth")
    sample_n = lax.axis_size("sample")
    total = flat.shape[0]
    per_depth = total // depth_n
    per_all = per_depth // sample_n
    step = lax.all_to_all(flat.reshape(depth_n, per_depth), "depth", 0, 0, tiled=True).sum(0)
    step = lax.all_to_all(step.reshape(sample_n, per_all), "sample", 0, 0, tiled=True).sum(0)
    step = lax.all_to_all(jnp.broadcast_to(step[None], (sample_n, per_all)), "sample", 0, 0, tiled=True)
    step = lax.all_to_all(
        jnp.broadcast_to(step.reshape(1, per_depth), (depth_n, per_depth)), "depth", 0, 0, tiled=True
    ).reshape(total)
    out = []
    start = 0
    for p in parts:
        out.append(step[start : start + p.size].reshape(p.shape))
        start += p.size
    return tuple(out)


def tap_shift(cells, along_z, along_y, along_x, slabs_n, rows_n, cols_n):
    return cells[
        :,
        along_z : along_z + slabs_n,
        along_y : along_y + rows_n,
        along_x : along_x + cols_n,
    ]


def mid_back(in_padded, cot_padded, kernel, deep_part, slabs_n, rows_n, cols_n):
    center = cot_padded[:, 1 : 1 + slabs_n, 1 : 1 + rows_n, 1 : 1 + cols_n]
    taps = [(z, y, x) for z in range(3) for y in range(3) for x in range(3)]
    pieces = [
        jnp.einsum(
            "czhw,ozhw->co",
            tap_shift(in_padded, z, y, x, slabs_n, rows_n, cols_n),
            center,
            preferred_element_type=jnp.float32,
        )
        for z, y, x in taps
    ]
    mid_part = jnp.stack(pieces)

    def add_taps(data_part, cot_now, chosen):
        for z, y, x in chosen:
            moved = tap_shift(cot_now, 2 - z, 2 - y, 2 - x, slabs_n, rows_n, cols_n)
            data_part = data_part + jnp.einsum(
                "co,ozhw->czhw", kernel[(z * 3 + y) * 3 + x], moved, preferred_element_type=jnp.float32
            )
        return data_part

    parts = (deep_part, mid_part)
    flat = jnp.concatenate([p.reshape(-1) for p in parts])
    first_n = lax.axis_size("sample")
    second_n = lax.axis_size("depth")
    total = flat.shape[0]
    per_first = total // first_n
    per_all = per_first // second_n
    data_part = jnp.zeros((in_padded.shape[0], slabs_n, rows_n, cols_n), jnp.float32)
    step = lax.all_to_all(flat.reshape(first_n, per_first), "sample", 0, 0, tiled=True)
    data_part = add_taps(data_part, cot_padded, taps[0:10])
    step, data_part, cot_now = lax.optimization_barrier((step, data_part, cot_padded))
    step = lax.all_to_all(step.sum(0).reshape(second_n, per_all), "depth", 0, 0, tiled=True)
    data_part = add_taps(data_part, cot_now, taps[10:14])
    step, data_part, cot_now = lax.optimization_barrier((step, data_part, cot_padded))
    step = lax.all_to_all(jnp.broadcast_to(step.sum(0)[None], (second_n, per_all)), "depth", 0, 0, tiled=True)
    data_part = add_taps(data_part, cot_now, taps[14:18])
    step, data_part, cot_now = lax.optimization_barrier((step, data_part, cot_padded))
    step = lax.all_to_all(
        jnp.broadcast_to(step.reshape(1, per_first), (first_n, per_first)), "sample", 0, 0, tiled=True
    ).reshape(total)
    data_part = add_taps(data_part, cot_now, taps[18:27])
    sums = []
    start = 0
    for p in parts:
        sums.append(step[start : start + p.size].reshape(p.shape))
        start += p.size
    return sums[0], sums[1], data_part


def body(layer_input, preact, cotangent, kernel_mid, kernel_deep):
    input_slab = layer_input[0]
    preact_slab = preact[0]
    deep_cot = cotangent[0]
    chan_mid, slabs_n, rows_n, cols_n = preact_slab.shape
    input_halo = padded(input_slab, (("depth", 1),), 1)
    input_padded = pad_spatial(input_halo, 1)
    preact_f32 = preact_slab.astype(jnp.float32)
    activated = jnp.where(preact_f32 > 0, preact_f32, leak_slope * preact_f32)
    pooled = (
        activated.reshape(chan_mid, slabs_n // 2, 2, rows_n // 2, 2, cols_n // 2, 2)
        .mean(axis=(2, 4, 6))
        .astype(jnp.bfloat16)
    )
    slab_cot = lax.all_to_all(deep_cot, "depth", split_axis=1, concat_axis=2, tiled=True)
    joined = jnp.concatenate([pooled, slab_cot], axis=0)
    joined_halo = padded(joined, (("depth", 1),), 1)
    joined_pad = pad_spatial(joined_halo, 1)
    deep_part, deep_data = local_back(
        joined_pad[:chan_mid],
        joined_pad[chan_mid:],
        kernel_deep,
        slabs_n // 2,
        rows_n // 2,
        cols_n // 2,
    )
    deep_data = deep_data.astype(jnp.bfloat16)
    expanded = jnp.broadcast_to(
        deep_data[:, :, None, :, None, :, None],
        (chan_mid, slabs_n // 2, 2, rows_n // 2, 2, cols_n // 2, 2),
    ).reshape(chan_mid, slabs_n, rows_n, cols_n)
    mid_cot = (
        expanded.astype(jnp.float32) * 0.125 * jnp.where(preact_f32 > 0, 1.0, leak_slope)
    ).astype(jnp.bfloat16)
    cot_halo = padded(mid_cot, (("depth", 1),), 1)
    deep_sum, mid_sum, data_part = mid_back(
        input_padded, pad_spatial(cot_halo, 1), kernel_mid, deep_part, slabs_n, rows_n, cols_n
    )
    cells = lax.axis_size("sample") * lax.axis_size("depth") * slabs_n * rows_n * cols_n
    grad_mid = mid_sum * (1.0 / math.sqrt(cells))
    grad_deep = deep_sum * (1.0 / math.sqrt(cells / 8))
    return (grad_mid, grad_deep, data_part.astype(jnp.bfloat16)[None])


def solution(mesh):
    return jax.shard_map(
        body,
        mesh=mesh,
        in_specs=(
            P("sample", None, "depth", None, None),
            P("sample", None, "depth", None, None),
            P("sample", None, None, "depth", None),
            P(),
            P(),
        ),
        out_specs=(P(), P(), P("sample", None, "depth", None, None)),
        check_vma=False,
    )
```

```python
import math

import jax
import jax.numpy as jnp
from jax import lax
from jax.sharding import PartitionSpec as P

leak_slope = 0.3


def padded(cells, sides, width):
    for axis, dim in sides:
        count = lax.axis_size(axis)
        ends = count - 1
        head = lax.slice_in_dim(cells, 0, width, axis=dim)
        tail = lax.slice_in_dim(cells, cells.shape[dim] - width, cells.shape[dim], axis=dim)
        cells = jnp.concatenate(
            [
                lax.ppermute(tail, axis, [(i, (i + 1) % count) for i in range(ends)]),
                cells,
                lax.ppermute(head, axis, [((i + 1) % count, i) for i in range(ends)]),
            ],
            axis=dim,
        )
    return cells


def padded_together(first, second, axis, dim):
    count = lax.axis_size(axis)
    ends = count - 1
    arrays = (first, second)
    heads = [lax.slice_in_dim(a, 0, 1, axis=dim) for a in arrays]
    tails = [lax.slice_in_dim(a, a.shape[dim] - 1, a.shape[dim], axis=dim) for a in arrays]
    sent_tails = lax.ppermute(
        jnp.concatenate([t.reshape(-1) for t in tails]), axis, [(i, (i + 1) % count) for i in range(ends)]
    )
    sent_heads = lax.ppermute(
        jnp.concatenate([h.reshape(-1) for h in heads]), axis, [((i + 1) % count, i) for i in range(ends)]
    )
    out = []
    start = 0
    for a, h, t in zip(arrays, heads, tails):
        size = h.size
        before = sent_tails[start : start + size].reshape(t.shape)
        after = sent_heads[start : start + size].reshape(h.shape)
        out.append(jnp.concatenate([before, a, after], axis=dim))
        start += size
    return tuple(out)


def pad_spatial(volume, halo_dim):
    widths = [(0, 0), (1, 1), (1, 1), (1, 1)]
    widths[halo_dim] = (0, 0)
    return jnp.pad(volume, widths)


def local_back(in_padded, cot_padded, kernel, slabs_n, rows_n, cols_n):
    center = cot_padded[:, 1 : 1 + slabs_n, 1 : 1 + rows_n, 1 : 1 + cols_n]
    data_part = jnp.zeros((in_padded.shape[0], slabs_n, rows_n, cols_n), jnp.float32)
    pieces = []
    for along_z in range(3):
        for along_y in range(3):
            for along_x in range(3):
                offset = (along_z * 3 + along_y) * 3 + along_x
                shifted = in_padded[
                    :,
                    along_z : along_z + slabs_n,
                    along_y : along_y + rows_n,
                    along_x : along_x + cols_n,
                ]
                pieces.append(
                    jnp.einsum("czhw,ozhw->co", shifted, center, preferred_element_type=jnp.float32)
                )
                moved = cot_padded[
                    :,
                    2 - along_z : 2 - along_z + slabs_n,
                    2 - along_y : 2 - along_y + rows_n,
                    2 - along_x : 2 - along_x + cols_n,
                ]
                data_part = data_part + jnp.einsum(
                    "co,ozhw->czhw", kernel[offset], moved, preferred_element_type=jnp.float32
                )
    return (jnp.stack(pieces), data_part)


def summed_everywhere(parts):
    flat = jnp.concatenate([p.reshape(-1) for p in parts])
    depth_n = lax.axis_size("depth")
    sample_n = lax.axis_size("sample")
    total = flat.shape[0]
    per_depth = total // depth_n
    per_all = per_depth // sample_n
    step = lax.all_to_all(flat.reshape(depth_n, per_depth), "depth", 0, 0, tiled=True).sum(0)
    step = lax.all_to_all(step.reshape(sample_n, per_all), "sample", 0, 0, tiled=True).sum(0)
    step = lax.all_to_all(jnp.broadcast_to(step[None], (sample_n, per_all)), "sample", 0, 0, tiled=True)
    step = lax.all_to_all(
        jnp.broadcast_to(step.reshape(1, per_depth), (depth_n, per_depth)), "depth", 0, 0, tiled=True
    ).reshape(total)
    out = []
    start = 0
    for p in parts:
        out.append(step[start : start + p.size].reshape(p.shape))
        start += p.size
    return tuple(out)


def tap_shift(cells, along_z, along_y, along_x, slabs_n, rows_n, cols_n):
    return cells[
        :,
        along_z : along_z + slabs_n,
        along_y : along_y + rows_n,
        along_x : along_x + cols_n,
    ]


def mid_back(in_padded, cot_padded, kernel, deep_part, slabs_n, rows_n, cols_n):
    center = cot_padded[:, 1 : 1 + slabs_n, 1 : 1 + rows_n, 1 : 1 + cols_n]
    taps = [(z, y, x) for z in range(3) for y in range(3) for x in range(3)]
    pieces = [
        jnp.einsum(
            "czhw,ozhw->co",
            tap_shift(in_padded, z, y, x, slabs_n, rows_n, cols_n),
            center,
            preferred_element_type=jnp.float32,
        )
        for z, y, x in taps
    ]
    mid_part = jnp.stack(pieces)

    def add_taps(data_part, cot_now, chosen):
        for z, y, x in chosen:
            moved = tap_shift(cot_now, 2 - z, 2 - y, 2 - x, slabs_n, rows_n, cols_n)
            data_part = data_part + jnp.einsum(
                "co,ozhw->czhw", kernel[(z * 3 + y) * 3 + x], moved, preferred_element_type=jnp.float32
            )
        return data_part

    parts = (deep_part, mid_part)
    flat = jnp.concatenate([p.reshape(-1) for p in parts])
    first_n = lax.axis_size("sample")
    second_n = lax.axis_size("depth")
    total = flat.shape[0]
    per_first = total // first_n
    per_all = per_first // second_n
    data_part = jnp.zeros((in_padded.shape[0], slabs_n, rows_n, cols_n), jnp.float32)
    step = lax.all_to_all(flat.reshape(first_n, per_first), "sample", 0, 0, tiled=True)
    data_part = add_taps(data_part, cot_padded, taps[0:10])
    step, data_part, cot_now = lax.optimization_barrier((step, data_part, cot_padded))
    step = lax.all_to_all(step.sum(0).reshape(second_n, per_all), "depth", 0, 0, tiled=True)
    data_part = add_taps(data_part, cot_now, taps[10:14])
    step, data_part, cot_now = lax.optimization_barrier((step, data_part, cot_padded))
    step = lax.all_to_all(jnp.broadcast_to(step.sum(0)[None], (second_n, per_all)), "depth", 0, 0, tiled=True)
    data_part = add_taps(data_part, cot_now, taps[14:18])
    step, data_part, cot_now = lax.optimization_barrier((step, data_part, cot_padded))
    step = lax.all_to_all(
        jnp.broadcast_to(step.reshape(1, per_first), (first_n, per_first)), "sample", 0, 0, tiled=True
    ).reshape(total)
    data_part = add_taps(data_part, cot_now, taps[18:27])
    sums = []
    start = 0
    for p in parts:
        sums.append(step[start : start + p.size].reshape(p.shape))
        start += p.size
    return sums[0], sums[1], data_part


def body(layer_input, preact, cotangent, kernel_mid, kernel_deep):
    input_slab = layer_input[0]
    preact_slab = preact[0]
    deep_cot = cotangent[0]
    chan_mid, slabs_n, rows_n, cols_n = preact_slab.shape
    preact_f32 = preact_slab.astype(jnp.float32)
    activated = jnp.where(preact_f32 > 0, preact_f32, leak_slope * preact_f32)
    pooled = (
        activated.reshape(chan_mid, slabs_n // 2, 2, rows_n // 2, 2, cols_n // 2, 2)
        .mean(axis=(2, 4, 6))
        .astype(jnp.bfloat16)
    )
    slab_cot = lax.all_to_all(deep_cot, "depth", split_axis=1, concat_axis=2, tiled=True)
    joined = jnp.concatenate([pooled, slab_cot], axis=0)
    input_halo, joined_halo = padded_together(input_slab, joined, "depth", 1)
    input_padded = pad_spatial(input_halo, 1)
    joined_pad = pad_spatial(joined_halo, 1)
    deep_part, deep_data = local_back(
        joined_pad[:chan_mid],
        joined_pad[chan_mid:],
        kernel_deep,
        slabs_n // 2,
        rows_n // 2,
        cols_n // 2,
    )
    deep_data = deep_data.astype(jnp.bfloat16)
    expanded = jnp.broadcast_to(
        deep_data[:, :, None, :, None, :, None],
        (chan_mid, slabs_n // 2, 2, rows_n // 2, 2, cols_n // 2, 2),
    ).reshape(chan_mid, slabs_n, rows_n, cols_n)
    mid_cot = (
        expanded.astype(jnp.float32) * 0.125 * jnp.where(preact_f32 > 0, 1.0, leak_slope)
    ).astype(jnp.bfloat16)
    cot_halo = padded(mid_cot, (("depth", 1),), 1)
    deep_sum, mid_sum, data_part = mid_back(
        input_padded, pad_spatial(cot_halo, 1), kernel_mid, deep_part, slabs_n, rows_n, cols_n
    )
    cells = lax.axis_size("sample") * lax.axis_size("depth") * slabs_n * rows_n * cols_n
    grad_mid = mid_sum * (1.0 / math.sqrt(cells))
    grad_deep = deep_sum * (1.0 / math.sqrt(cells / 8))
    return (grad_mid, grad_deep, data_part.astype(jnp.bfloat16)[None])


def solution(mesh):
    return jax.shard_map(
        body,
        mesh=mesh,
        in_specs=(
            P("sample", None, "depth", None, None),
            P("sample", None, "depth", None, None),
            P("sample", None, None, "depth", None),
            P(),
            P(),
        ),
        out_specs=(P(), P(), P("sample", None, "depth", None, None)),
        check_vma=False,
    )
```

```python
import math

import jax
import jax.numpy as jnp
from jax import lax
from jax.sharding import PartitionSpec as P

leak_slope = 0.3


def padded(cells, sides, width):
    for axis, dim in sides:
        count = lax.axis_size(axis)
        ends = count - 1
        head = lax.slice_in_dim(cells, 0, width, axis=dim)
        tail = lax.slice_in_dim(cells, cells.shape[dim] - width, cells.shape[dim], axis=dim)
        cells = jnp.concatenate(
            [
                lax.ppermute(tail, axis, [(i, (i + 1) % count) for i in range(ends)]),
                cells,
                lax.ppermute(head, axis, [((i + 1) % count, i) for i in range(ends)]),
            ],
            axis=dim,
        )
    return cells


def pad_spatial(volume, halo_dim):
    widths = [(0, 0), (1, 1), (1, 1), (1, 1)]
    widths[halo_dim] = (0, 0)
    return jnp.pad(volume, widths)


def local_back(in_padded, cot_padded, kernel, slabs_n, rows_n, cols_n):
    center = cot_padded[:, 1 : 1 + slabs_n, 1 : 1 + rows_n, 1 : 1 + cols_n]
    data_part = jnp.zeros((in_padded.shape[0], slabs_n, rows_n, cols_n), jnp.float32)
    pieces = []
    for along_z in range(3):
        for along_y in range(3):
            for along_x in range(3):
                offset = (along_z * 3 + along_y) * 3 + along_x
                shifted = in_padded[
                    :,
                    along_z : along_z + slabs_n,
                    along_y : along_y + rows_n,
                    along_x : along_x + cols_n,
                ]
                pieces.append(
                    jnp.einsum("czhw,ozhw->co", shifted, center, preferred_element_type=jnp.float32)
                )
                moved = cot_padded[
                    :,
                    2 - along_z : 2 - along_z + slabs_n,
                    2 - along_y : 2 - along_y + rows_n,
                    2 - along_x : 2 - along_x + cols_n,
                ]
                data_part = data_part + jnp.einsum(
                    "co,ozhw->czhw", kernel[offset], moved, preferred_element_type=jnp.float32
                )
    return (jnp.stack(pieces), data_part)


def summed_everywhere(parts):
    flat = jnp.concatenate([p.reshape(-1) for p in parts])
    depth_n = lax.axis_size("depth")
    sample_n = lax.axis_size("sample")
    total = flat.shape[0]
    per_depth = total // depth_n
    per_all = per_depth // sample_n
    step = lax.all_to_all(flat.reshape(depth_n, per_depth), "depth", 0, 0, tiled=True).sum(0)
    step = lax.all_to_all(step.reshape(sample_n, per_all), "sample", 0, 0, tiled=True).sum(0)
    step = lax.all_to_all(jnp.broadcast_to(step[None], (sample_n, per_all)), "sample", 0, 0, tiled=True)
    step = lax.all_to_all(
        jnp.broadcast_to(step.reshape(1, per_depth), (depth_n, per_depth)), "depth", 0, 0, tiled=True
    ).reshape(total)
    out = []
    start = 0
    for p in parts:
        out.append(step[start : start + p.size].reshape(p.shape))
        start += p.size
    return tuple(out)


def tap_shift(cells, along_z, along_y, along_x, slabs_n, rows_n, cols_n):
    return cells[
        :,
        along_z : along_z + slabs_n,
        along_y : along_y + rows_n,
        along_x : along_x + cols_n,
    ]


def mid_back(in_padded, cot_padded, kernel, deep_part, slabs_n, rows_n, cols_n):
    center = cot_padded[:, 1 : 1 + slabs_n, 1 : 1 + rows_n, 1 : 1 + cols_n]
    taps = [(z, y, x) for z in range(3) for y in range(3) for x in range(3)]
    by_column = jnp.stack([in_padded[:, :, :, x : x + cols_n] for x in range(3)])
    pieces = [
        jnp.einsum(
            "xczhw,ozhw->xco",
            by_column[:, :, z : z + slabs_n, y : y + rows_n, :],
            center,
            preferred_element_type=jnp.float32,
        )
        for z in range(3)
        for y in range(3)
    ]
    mid_part = jnp.concatenate(pieces)

    def add_taps(data_part, cot_now, chosen):
        for z, y, x in chosen:
            moved = tap_shift(cot_now, 2 - z, 2 - y, 2 - x, slabs_n, rows_n, cols_n)
            data_part = data_part + jnp.einsum(
                "co,ozhw->czhw", kernel[(z * 3 + y) * 3 + x], moved, preferred_element_type=jnp.float32
            )
        return data_part

    parts = (deep_part, mid_part)
    flat = jnp.concatenate([p.reshape(-1) for p in parts])
    first_n = lax.axis_size("sample")
    second_n = lax.axis_size("depth")
    total = flat.shape[0]
    per_first = total // first_n
    per_all = per_first // second_n
    data_part = jnp.zeros((in_padded.shape[0], slabs_n, rows_n, cols_n), jnp.float32)
    step = lax.all_to_all(flat.reshape(first_n, per_first), "sample", 0, 0, tiled=True)
    data_part = add_taps(data_part, cot_padded, taps[0:10])
    step, data_part, cot_now = lax.optimization_barrier((step, data_part, cot_padded))
    step = lax.all_to_all(step.sum(0).reshape(second_n, per_all), "depth", 0, 0, tiled=True)
    data_part = add_taps(data_part, cot_now, taps[10:14])
    step, data_part, cot_now = lax.optimization_barrier((step, data_part, cot_padded))
    step = lax.all_to_all(jnp.broadcast_to(step.sum(0)[None], (second_n, per_all)), "depth", 0, 0, tiled=True)
    data_part = add_taps(data_part, cot_now, taps[14:18])
    step, data_part, cot_now = lax.optimization_barrier((step, data_part, cot_padded))
    step = lax.all_to_all(
        jnp.broadcast_to(step.reshape(1, per_first), (first_n, per_first)), "sample", 0, 0, tiled=True
    ).reshape(total)
    data_part = add_taps(data_part, cot_now, taps[18:27])
    sums = []
    start = 0
    for p in parts:
        sums.append(step[start : start + p.size].reshape(p.shape))
        start += p.size
    return sums[0], sums[1], data_part


def body(layer_input, preact, cotangent, kernel_mid, kernel_deep):
    input_slab = layer_input[0]
    preact_slab = preact[0]
    deep_cot = cotangent[0]
    chan_mid, slabs_n, rows_n, cols_n = preact_slab.shape
    input_halo = padded(input_slab, (("depth", 1),), 1)
    input_padded = pad_spatial(input_halo, 1)
    preact_f32 = preact_slab.astype(jnp.float32)
    activated = jnp.where(preact_f32 > 0, preact_f32, leak_slope * preact_f32)
    pooled = (
        activated.reshape(chan_mid, slabs_n // 2, 2, rows_n // 2, 2, cols_n // 2, 2)
        .mean(axis=(2, 4, 6))
        .astype(jnp.bfloat16)
    )
    slab_cot = lax.all_to_all(deep_cot, "depth", split_axis=1, concat_axis=2, tiled=True)
    joined = jnp.concatenate([pooled, slab_cot], axis=0)
    joined_halo = padded(joined, (("depth", 1),), 1)
    joined_pad = pad_spatial(joined_halo, 1)
    deep_part, deep_data = local_back(
        joined_pad[:chan_mid],
        joined_pad[chan_mid:],
        kernel_deep,
        slabs_n // 2,
        rows_n // 2,
        cols_n // 2,
    )
    deep_data = deep_data.astype(jnp.bfloat16)
    expanded = jnp.broadcast_to(
        deep_data[:, :, None, :, None, :, None],
        (chan_mid, slabs_n // 2, 2, rows_n // 2, 2, cols_n // 2, 2),
    ).reshape(chan_mid, slabs_n, rows_n, cols_n)
    mid_cot = (
        expanded.astype(jnp.float32) * 0.125 * jnp.where(preact_f32 > 0, 1.0, leak_slope)
    ).astype(jnp.bfloat16)
    cot_halo = padded(mid_cot, (("depth", 1),), 1)
    deep_sum, mid_sum, data_part = mid_back(
        input_padded, pad_spatial(cot_halo, 1), kernel_mid, deep_part, slabs_n, rows_n, cols_n
    )
    cells = lax.axis_size("sample") * lax.axis_size("depth") * slabs_n * rows_n * cols_n
    grad_mid = mid_sum * (1.0 / math.sqrt(cells))
    grad_deep = deep_sum * (1.0 / math.sqrt(cells / 8))
    return (grad_mid, grad_deep, data_part.astype(jnp.bfloat16)[None])


def solution(mesh):
    return jax.shard_map(
        body,
        mesh=mesh,
        in_specs=(
            P("sample", None, "depth", None, None),
            P("sample", None, "depth", None, None),
            P("sample", None, None, "depth", None),
            P(),
            P(),
        ),
        out_specs=(P(), P(), P("sample", None, "depth", None, None)),
        check_vma=False,
    )
```

```python
import math

import jax
import jax.numpy as jnp
from jax import lax
from jax.sharding import PartitionSpec as P

leak_slope = 0.3


def padded(cells, sides, width):
    for axis, dim in sides:
        count = lax.axis_size(axis)
        ends = count - 1
        head = lax.slice_in_dim(cells, 0, width, axis=dim)
        tail = lax.slice_in_dim(cells, cells.shape[dim] - width, cells.shape[dim], axis=dim)
        cells = jnp.concatenate(
            [
                lax.ppermute(tail, axis, [(i, (i + 1) % count) for i in range(ends)]),
                cells,
                lax.ppermute(head, axis, [((i + 1) % count, i) for i in range(ends)]),
            ],
            axis=dim,
        )
    return cells


def pad_spatial(volume, halo_dim):
    widths = [(0, 0), (1, 1), (1, 1), (1, 1)]
    widths[halo_dim] = (0, 0)
    return jnp.pad(volume, widths)


def local_back(in_padded, cot_padded, kernel, slabs_n, rows_n, cols_n):
    center = cot_padded[:, 1 : 1 + slabs_n, 1 : 1 + rows_n, 1 : 1 + cols_n]
    by_column = jnp.stack([in_padded[:, :, :, x : x + cols_n] for x in range(3)])
    cot_columns = jnp.stack([cot_padded[:, :, :, 2 - x : 2 - x + cols_n] for x in range(3)])
    per_row = kernel.reshape(3, 3, 3, kernel.shape[1], kernel.shape[2])
    data_part = jnp.zeros((in_padded.shape[0], slabs_n, rows_n, cols_n), jnp.float32)
    pieces = []
    for along_z in range(3):
        for along_y in range(3):
            pieces.append(
                jnp.einsum(
                    "xczhw,ozhw->xco",
                    by_column[:, :, along_z : along_z + slabs_n, along_y : along_y + rows_n, :],
                    center,
                    preferred_element_type=jnp.float32,
                )
            )
            moved = cot_columns[:, :, 2 - along_z : 2 - along_z + slabs_n, 2 - along_y : 2 - along_y + rows_n, :]
            data_part = data_part + jnp.einsum(
                "xco,xozhw->czhw", per_row[along_z, along_y], moved, preferred_element_type=jnp.float32
            )
    return (jnp.concatenate(pieces), data_part)


def summed_everywhere(parts):
    flat = jnp.concatenate([p.reshape(-1) for p in parts])
    depth_n = lax.axis_size("depth")
    sample_n = lax.axis_size("sample")
    total = flat.shape[0]
    per_depth = total // depth_n
    per_all = per_depth // sample_n
    step = lax.all_to_all(flat.reshape(depth_n, per_depth), "depth", 0, 0, tiled=True).sum(0)
    step = lax.all_to_all(step.reshape(sample_n, per_all), "sample", 0, 0, tiled=True).sum(0)
    step = lax.all_to_all(jnp.broadcast_to(step[None], (sample_n, per_all)), "sample", 0, 0, tiled=True)
    step = lax.all_to_all(
        jnp.broadcast_to(step.reshape(1, per_depth), (depth_n, per_depth)), "depth", 0, 0, tiled=True
    ).reshape(total)
    out = []
    start = 0
    for p in parts:
        out.append(step[start : start + p.size].reshape(p.shape))
        start += p.size
    return tuple(out)


def mid_back(in_padded, cot_padded, kernel, deep_part, slabs_n, rows_n, cols_n):
    center = cot_padded[:, 1 : 1 + slabs_n, 1 : 1 + rows_n, 1 : 1 + cols_n]
    by_column = jnp.stack([in_padded[:, :, :, x : x + cols_n] for x in range(3)])
    pieces = [
        jnp.einsum(
            "xczhw,ozhw->xco",
            by_column[:, :, z : z + slabs_n, y : y + rows_n, :],
            center,
            preferred_element_type=jnp.float32,
        )
        for z in range(3)
        for y in range(3)
    ]
    mid_part = jnp.concatenate(pieces)

    per_row = kernel.reshape(3, 3, 3, kernel.shape[1], kernel.shape[2])
    rows = [(z, y) for z in range(3) for y in range(3)]

    def add_taps(data_part, cot_now, chosen):
        for z, y in chosen:
            moved = cot_now[:, :, 2 - z : 2 - z + slabs_n, 2 - y : 2 - y + rows_n, :]
            data_part = data_part + jnp.einsum(
                "xco,xozhw->czhw", per_row[z, y], moved, preferred_element_type=jnp.float32
            )
        return data_part

    parts = (deep_part, mid_part)
    flat = jnp.concatenate([p.reshape(-1) for p in parts])
    first_n = lax.axis_size("sample")
    second_n = lax.axis_size("depth")
    total = flat.shape[0]
    per_first = total // first_n
    per_all = per_first // second_n
    data_part = jnp.zeros((in_padded.shape[0], slabs_n, rows_n, cols_n), jnp.float32)
    cot_columns = jnp.stack([cot_padded[:, :, :, 2 - x : 2 - x + cols_n] for x in range(3)])
    step = lax.all_to_all(flat.reshape(first_n, per_first), "sample", 0, 0, tiled=True)
    data_part = add_taps(data_part, cot_columns, rows[0:3])
    step, data_part, cot_now = lax.optimization_barrier((step, data_part, cot_columns))
    step = lax.all_to_all(step.sum(0).reshape(second_n, per_all), "depth", 0, 0, tiled=True)
    data_part = add_taps(data_part, cot_now, rows[3:5])
    step, data_part, cot_now = lax.optimization_barrier((step, data_part, cot_columns))
    step = lax.all_to_all(jnp.broadcast_to(step.sum(0)[None], (second_n, per_all)), "depth", 0, 0, tiled=True)
    data_part = add_taps(data_part, cot_now, rows[5:7])
    step, data_part, cot_now = lax.optimization_barrier((step, data_part, cot_columns))
    step = lax.all_to_all(
        jnp.broadcast_to(step.reshape(1, per_first), (first_n, per_first)), "sample", 0, 0, tiled=True
    ).reshape(total)
    data_part = add_taps(data_part, cot_now, rows[7:9])
    sums = []
    start = 0
    for p in parts:
        sums.append(step[start : start + p.size].reshape(p.shape))
        start += p.size
    return sums[0], sums[1], data_part


def body(layer_input, preact, cotangent, kernel_mid, kernel_deep):
    input_slab = layer_input[0]
    preact_slab = preact[0]
    deep_cot = cotangent[0]
    chan_mid, slabs_n, rows_n, cols_n = preact_slab.shape
    input_halo = padded(input_slab, (("depth", 1),), 1)
    input_padded = pad_spatial(input_halo, 1)
    preact_f32 = preact_slab.astype(jnp.float32)
    activated = jnp.where(preact_f32 > 0, preact_f32, leak_slope * preact_f32)
    pooled = (
        activated.reshape(chan_mid, slabs_n // 2, 2, rows_n // 2, 2, cols_n // 2, 2)
        .mean(axis=(2, 4, 6))
        .astype(jnp.bfloat16)
    )
    slab_cot = lax.all_to_all(deep_cot, "depth", split_axis=1, concat_axis=2, tiled=True)
    joined = jnp.concatenate([pooled, slab_cot], axis=0)
    joined_halo = padded(joined, (("depth", 1),), 1)
    joined_pad = pad_spatial(joined_halo, 1)
    deep_part, deep_data = local_back(
        joined_pad[:chan_mid],
        joined_pad[chan_mid:],
        kernel_deep,
        slabs_n // 2,
        rows_n // 2,
        cols_n // 2,
    )
    deep_data = deep_data.astype(jnp.bfloat16)
    expanded = jnp.broadcast_to(
        deep_data[:, :, None, :, None, :, None],
        (chan_mid, slabs_n // 2, 2, rows_n // 2, 2, cols_n // 2, 2),
    ).reshape(chan_mid, slabs_n, rows_n, cols_n)
    mid_cot = (
        expanded.astype(jnp.float32) * 0.125 * jnp.where(preact_f32 > 0, 1.0, leak_slope)
    ).astype(jnp.bfloat16)
    cot_halo = padded(mid_cot, (("depth", 1),), 1)
    deep_sum, mid_sum, data_part = mid_back(
        input_padded, pad_spatial(cot_halo, 1), kernel_mid, deep_part, slabs_n, rows_n, cols_n
    )
    cells = lax.axis_size("sample") * lax.axis_size("depth") * slabs_n * rows_n * cols_n
    grad_mid = mid_sum * (1.0 / math.sqrt(cells))
    grad_deep = deep_sum * (1.0 / math.sqrt(cells / 8))
    return (grad_mid, grad_deep, data_part.astype(jnp.bfloat16)[None])


def solution(mesh):
    return jax.shard_map(
        body,
        mesh=mesh,
        in_specs=(
            P("sample", None, "depth", None, None),
            P("sample", None, "depth", None, None),
            P("sample", None, None, "depth", None),
            P(),
            P(),
        ),
        out_specs=(P(), P(), P("sample", None, "depth", None, None)),
        check_vma=False,
    )
```

```python
import math

import jax
import jax.numpy as jnp
from jax import lax
from jax.sharding import PartitionSpec as P

leak_slope = 0.3


def padded(cells, sides, width):
    for axis, dim in sides:
        count = lax.axis_size(axis)
        ends = count - 1
        head = lax.slice_in_dim(cells, 0, width, axis=dim)
        tail = lax.slice_in_dim(cells, cells.shape[dim] - width, cells.shape[dim], axis=dim)
        cells = jnp.concatenate(
            [
                lax.ppermute(tail, axis, [(i, (i + 1) % count) for i in range(ends)]),
                cells,
                lax.ppermute(head, axis, [((i + 1) % count, i) for i in range(ends)]),
            ],
            axis=dim,
        )
    return cells


def pad_spatial(volume, halo_dim):
    widths = [(0, 0), (1, 1), (1, 1), (1, 1)]
    widths[halo_dim] = (0, 0)
    return jnp.pad(volume, widths)


def local_back(in_padded, cot_padded, kernel, slabs_n, rows_n, cols_n):
    center = cot_padded[:, 1 : 1 + slabs_n, 1 : 1 + rows_n, 1 : 1 + cols_n]
    by_column = jnp.stack([in_padded[:, :, :, x : x + cols_n] for x in range(3)])
    cot_columns = jnp.stack([cot_padded[:, :, :, 2 - x : 2 - x + cols_n] for x in range(3)])
    per_row = kernel.reshape(3, 3, 3, kernel.shape[1], kernel.shape[2])
    data_part = jnp.zeros((in_padded.shape[0], slabs_n, rows_n, cols_n), jnp.float32)
    pieces = []
    for along_z in range(3):
        for along_y in range(3):
            pieces.append(
                jnp.einsum(
                    "xczhw,ozhw->xco",
                    by_column[:, :, along_z : along_z + slabs_n, along_y : along_y + rows_n, :],
                    center,
                    preferred_element_type=jnp.float32,
                )
            )
            moved = cot_columns[:, :, 2 - along_z : 2 - along_z + slabs_n, 2 - along_y : 2 - along_y + rows_n, :]
            data_part = data_part + jnp.einsum(
                "xco,xozhw->czhw", per_row[along_z, along_y], moved, preferred_element_type=jnp.float32
            )
    return (jnp.concatenate(pieces), data_part)


def summed_everywhere(parts):
    flat = jnp.concatenate([p.reshape(-1) for p in parts])
    depth_n = lax.axis_size("depth")
    sample_n = lax.axis_size("sample")
    total = flat.shape[0]
    per_depth = total // depth_n
    per_all = per_depth // sample_n
    step = lax.all_to_all(flat.reshape(depth_n, per_depth), "depth", 0, 0, tiled=True).sum(0)
    step = lax.all_to_all(step.reshape(sample_n, per_all), "sample", 0, 0, tiled=True).sum(0)
    step = lax.all_to_all(jnp.broadcast_to(step[None], (sample_n, per_all)), "sample", 0, 0, tiled=True)
    step = lax.all_to_all(
        jnp.broadcast_to(step.reshape(1, per_depth), (depth_n, per_depth)), "depth", 0, 0, tiled=True
    ).reshape(total)
    out = []
    start = 0
    for p in parts:
        out.append(step[start : start + p.size].reshape(p.shape))
        start += p.size
    return tuple(out)


def mid_back(in_padded, cot_padded, kernel, deep_part, slabs_n, rows_n, cols_n):
    center = cot_padded[:, 1 : 1 + slabs_n, 1 : 1 + rows_n, 1 : 1 + cols_n]
    by_column = jnp.stack([in_padded[:, :, :, x : x + cols_n] for x in range(3)])
    pieces = [
        jnp.einsum(
            "xczhw,ozhw->xco",
            by_column[:, :, z : z + slabs_n, y : y + rows_n, :],
            center,
            preferred_element_type=jnp.float32,
        )
        for z in range(3)
        for y in range(3)
    ]
    mid_part = jnp.concatenate(pieces)

    per_row = kernel.reshape(3, 3, 3, kernel.shape[1], kernel.shape[2])
    rows = [(z, y) for z in range(3) for y in range(3)]

    def add_taps(data_part, cot_now, chosen):
        for z, y in chosen:
            moved = cot_now[:, :, 2 - z : 2 - z + slabs_n, 2 - y : 2 - y + rows_n, :]
            data_part = data_part + jnp.einsum(
                "xco,xozhw->czhw", per_row[z, y], moved, preferred_element_type=jnp.float32
            )
        return data_part

    parts = (deep_part, mid_part)
    flat = jnp.concatenate([p.reshape(-1) for p in parts])
    first_n = lax.axis_size("sample")
    second_n = lax.axis_size("depth")
    total = flat.shape[0]
    per_first = total // first_n
    per_all = per_first // second_n
    data_part = jnp.zeros((in_padded.shape[0], slabs_n, rows_n, cols_n), jnp.float32)
    cot_columns = jnp.stack([cot_padded[:, :, :, 2 - x : 2 - x + cols_n] for x in range(3)])
    step = lax.all_to_all(flat.reshape(first_n, per_first), "sample", 0, 0, tiled=True)
    data_part = add_taps(data_part, cot_columns, rows[0:3])
    step, data_part, cot_now = lax.optimization_barrier((step, data_part, cot_columns))
    step = lax.all_to_all(step.sum(0).reshape(second_n, per_all), "depth", 0, 0, tiled=True)
    data_part = add_taps(data_part, cot_now, rows[3:4])
    step, data_part, cot_now = lax.optimization_barrier((step, data_part, cot_columns))
    step = lax.all_to_all(jnp.broadcast_to(step.sum(0)[None], (second_n, per_all)), "depth", 0, 0, tiled=True)
    data_part = add_taps(data_part, cot_now, rows[4:6])
    step, data_part, cot_now = lax.optimization_barrier((step, data_part, cot_columns))
    step = lax.all_to_all(
        jnp.broadcast_to(step.reshape(1, per_first), (first_n, per_first)), "sample", 0, 0, tiled=True
    ).reshape(total)
    data_part = add_taps(data_part, cot_now, rows[6:9])
    sums = []
    start = 0
    for p in parts:
        sums.append(step[start : start + p.size].reshape(p.shape))
        start += p.size
    return sums[0], sums[1], data_part


def body(layer_input, preact, cotangent, kernel_mid, kernel_deep):
    input_slab = layer_input[0]
    preact_slab = preact[0]
    deep_cot = cotangent[0]
    chan_mid, slabs_n, rows_n, cols_n = preact_slab.shape
    input_halo = padded(input_slab, (("depth", 1),), 1)
    input_padded = pad_spatial(input_halo, 1)
    preact_f32 = preact_slab.astype(jnp.float32)
    activated = jnp.where(preact_f32 > 0, preact_f32, leak_slope * preact_f32)
    pooled = (
        activated.reshape(chan_mid, slabs_n // 2, 2, rows_n // 2, 2, cols_n // 2, 2)
        .mean(axis=(2, 4, 6))
        .astype(jnp.bfloat16)
    )
    slab_cot = lax.all_to_all(deep_cot, "depth", split_axis=1, concat_axis=2, tiled=True)
    joined = jnp.concatenate([pooled, slab_cot], axis=0)
    joined_halo = padded(joined, (("depth", 1),), 1)
    joined_pad = pad_spatial(joined_halo, 1)
    deep_part, deep_data = local_back(
        joined_pad[:chan_mid],
        joined_pad[chan_mid:],
        kernel_deep,
        slabs_n // 2,
        rows_n // 2,
        cols_n // 2,
    )
    deep_data = deep_data.astype(jnp.bfloat16)
    expanded = jnp.broadcast_to(
        deep_data[:, :, None, :, None, :, None],
        (chan_mid, slabs_n // 2, 2, rows_n // 2, 2, cols_n // 2, 2),
    ).reshape(chan_mid, slabs_n, rows_n, cols_n)
    mid_cot = (
        expanded.astype(jnp.float32) * 0.125 * jnp.where(preact_f32 > 0, 1.0, leak_slope)
    ).astype(jnp.bfloat16)
    cot_halo = padded(mid_cot, (("depth", 1),), 1)
    deep_sum, mid_sum, data_part = mid_back(
        input_padded, pad_spatial(cot_halo, 1), kernel_mid, deep_part, slabs_n, rows_n, cols_n
    )
    cells = lax.axis_size("sample") * lax.axis_size("depth") * slabs_n * rows_n * cols_n
    grad_mid = mid_sum * (1.0 / math.sqrt(cells))
    grad_deep = deep_sum * (1.0 / math.sqrt(cells / 8))
    return (grad_mid, grad_deep, data_part.astype(jnp.bfloat16)[None])


def solution(mesh):
    return jax.shard_map(
        body,
        mesh=mesh,
        in_specs=(
            P("sample", None, "depth", None, None),
            P("sample", None, "depth", None, None),
            P("sample", None, None, "depth", None),
            P(),
            P(),
        ),
        out_specs=(P(), P(), P("sample", None, "depth", None, None)),
        check_vma=False,
    )
```

```python
import math

import jax
import jax.numpy as jnp
from jax import lax
from jax.sharding import PartitionSpec as P

leak_slope = 0.3


def padded(cells, sides, width):
    for axis, dim in sides:
        count = lax.axis_size(axis)
        ends = count - 1
        head = lax.slice_in_dim(cells, 0, width, axis=dim)
        tail = lax.slice_in_dim(cells, cells.shape[dim] - width, cells.shape[dim], axis=dim)
        cells = jnp.concatenate(
            [
                lax.ppermute(tail, axis, [(i, (i + 1) % count) for i in range(ends)]),
                cells,
                lax.ppermute(head, axis, [((i + 1) % count, i) for i in range(ends)]),
            ],
            axis=dim,
        )
    return cells


def pad_spatial(volume, halo_dim):
    widths = [(0, 0), (1, 1), (1, 1), (1, 1)]
    widths[halo_dim] = (0, 0)
    return jnp.pad(volume, widths)


def local_back(in_padded, cot_padded, kernel, slabs_n, rows_n, cols_n):
    center = cot_padded[:, 1 : 1 + slabs_n, 1 : 1 + rows_n, 1 : 1 + cols_n]
    by_column = jnp.stack([in_padded[:, :, :, x : x + cols_n] for x in range(3)])
    cot_columns = jnp.stack([cot_padded[:, :, :, 2 - x : 2 - x + cols_n] for x in range(3)])
    per_row = kernel.reshape(3, 3, 3, kernel.shape[1], kernel.shape[2])
    data_part = jnp.zeros((in_padded.shape[0], slabs_n, rows_n, cols_n), jnp.float32)
    pieces = []
    for along_z in range(3):
        for along_y in range(3):
            pieces.append(
                jnp.einsum(
                    "xczhw,ozhw->xco",
                    by_column[:, :, along_z : along_z + slabs_n, along_y : along_y + rows_n, :],
                    center,
                    preferred_element_type=jnp.float32,
                )
            )
            moved = cot_columns[:, :, 2 - along_z : 2 - along_z + slabs_n, 2 - along_y : 2 - along_y + rows_n, :]
            data_part = data_part + jnp.einsum(
                "xco,xozhw->czhw", per_row[along_z, along_y], moved, preferred_element_type=jnp.float32
            )
    return (jnp.concatenate(pieces), data_part)


def summed_everywhere(parts):
    flat = jnp.concatenate([p.reshape(-1) for p in parts])
    depth_n = lax.axis_size("depth")
    sample_n = lax.axis_size("sample")
    total = flat.shape[0]
    per_depth = total // depth_n
    per_all = per_depth // sample_n
    step = lax.all_to_all(flat.reshape(depth_n, per_depth), "depth", 0, 0, tiled=True).sum(0)
    step = lax.all_to_all(step.reshape(sample_n, per_all), "sample", 0, 0, tiled=True).sum(0)
    step = lax.all_to_all(jnp.broadcast_to(step[None], (sample_n, per_all)), "sample", 0, 0, tiled=True)
    step = lax.all_to_all(
        jnp.broadcast_to(step.reshape(1, per_depth), (depth_n, per_depth)), "depth", 0, 0, tiled=True
    ).reshape(total)
    out = []
    start = 0
    for p in parts:
        out.append(step[start : start + p.size].reshape(p.shape))
        start += p.size
    return tuple(out)


def mid_back(in_padded, cot_padded, kernel, deep_part, slabs_n, rows_n, cols_n):
    center = cot_padded[:, 1 : 1 + slabs_n, 1 : 1 + rows_n, 1 : 1 + cols_n]
    by_column = jnp.stack([in_padded[:, :, :, x : x + cols_n] for x in range(3)])
    pieces = [
        jnp.einsum(
            "xczhw,ozhw->xco",
            by_column[:, :, z : z + slabs_n, y : y + rows_n, :],
            center,
            preferred_element_type=jnp.float32,
        )
        for z in range(3)
        for y in range(3)
    ]
    mid_part = jnp.concatenate(pieces)

    per_row = kernel.reshape(3, 3, 3, kernel.shape[1], kernel.shape[2])
    rows = [(z, y) for z in range(3) for y in range(3)]

    def add_taps(data_part, cot_now, chosen):
        for z, y in chosen:
            moved = cot_now[:, :, 2 - z : 2 - z + slabs_n, 2 - y : 2 - y + rows_n, :]
            data_part = data_part + jnp.einsum(
                "xco,xozhw->czhw", per_row[z, y], moved, preferred_element_type=jnp.float32
            )
        return data_part

    parts = (deep_part, mid_part)
    flat = jnp.concatenate([p.reshape(-1) for p in parts])
    first_n = lax.axis_size("sample")
    second_n = lax.axis_size("depth")
    total = flat.shape[0]
    per_first = total // first_n
    per_all = per_first // second_n
    data_part = jnp.zeros((in_padded.shape[0], slabs_n, rows_n, cols_n), jnp.float32)
    cot_columns = jnp.stack([cot_padded[:, :, :, 2 - x : 2 - x + cols_n] for x in range(3)])
    step = lax.all_to_all(flat.reshape(first_n, per_first), "sample", 0, 0, tiled=True)
    data_part = add_taps(data_part, cot_columns, rows[0:3])
    step, data_part, cot_now = lax.optimization_barrier((step, data_part, cot_columns))
    step = lax.all_to_all(step.sum(0).reshape(second_n, per_all), "depth", 0, 0, tiled=True)
    data_part = add_taps(data_part, cot_now, rows[3:4])
    step, data_part, cot_now = lax.optimization_barrier((step, data_part, cot_columns))
    step = lax.all_to_all(jnp.broadcast_to(step.sum(0)[None], (second_n, per_all)), "depth", 0, 0, tiled=True)
    data_part = add_taps(data_part, cot_now, rows[4:5])
    step, data_part, cot_now = lax.optimization_barrier((step, data_part, cot_columns))
    step = lax.all_to_all(
        jnp.broadcast_to(step.reshape(1, per_first), (first_n, per_first)), "sample", 0, 0, tiled=True
    ).reshape(total)
    data_part = add_taps(data_part, cot_now, rows[5:9])
    sums = []
    start = 0
    for p in parts:
        sums.append(step[start : start + p.size].reshape(p.shape))
        start += p.size
    return sums[0], sums[1], data_part


def body(layer_input, preact, cotangent, kernel_mid, kernel_deep):
    input_slab = layer_input[0]
    preact_slab = preact[0]
    deep_cot = cotangent[0]
    chan_mid, slabs_n, rows_n, cols_n = preact_slab.shape
    input_halo = padded(input_slab, (("depth", 1),), 1)
    input_padded = pad_spatial(input_halo, 1)
    preact_f32 = preact_slab.astype(jnp.float32)
    activated = jnp.where(preact_f32 > 0, preact_f32, leak_slope * preact_f32)
    pooled = (
        activated.reshape(chan_mid, slabs_n // 2, 2, rows_n // 2, 2, cols_n // 2, 2)
        .mean(axis=(2, 4, 6))
        .astype(jnp.bfloat16)
    )
    slab_cot = lax.all_to_all(deep_cot, "depth", split_axis=1, concat_axis=2, tiled=True)
    joined = jnp.concatenate([pooled, slab_cot], axis=0)
    joined_halo = padded(joined, (("depth", 1),), 1)
    joined_pad = pad_spatial(joined_halo, 1)
    deep_part, deep_data = local_back(
        joined_pad[:chan_mid],
        joined_pad[chan_mid:],
        kernel_deep,
        slabs_n // 2,
        rows_n // 2,
        cols_n // 2,
    )
    deep_data = deep_data.astype(jnp.bfloat16)
    expanded = jnp.broadcast_to(
        deep_data[:, :, None, :, None, :, None],
        (chan_mid, slabs_n // 2, 2, rows_n // 2, 2, cols_n // 2, 2),
    ).reshape(chan_mid, slabs_n, rows_n, cols_n)
    mid_cot = (
        expanded.astype(jnp.float32) * 0.125 * jnp.where(preact_f32 > 0, 1.0, leak_slope)
    ).astype(jnp.bfloat16)
    cot_halo = padded(mid_cot, (("depth", 1),), 1)
    deep_sum, mid_sum, data_part = mid_back(
        input_padded, pad_spatial(cot_halo, 1), kernel_mid, deep_part, slabs_n, rows_n, cols_n
    )
    cells = lax.axis_size("sample") * lax.axis_size("depth") * slabs_n * rows_n * cols_n
    grad_mid = mid_sum * (1.0 / math.sqrt(cells))
    grad_deep = deep_sum * (1.0 / math.sqrt(cells / 8))
    return (grad_mid, grad_deep, data_part.astype(jnp.bfloat16)[None])


def solution(mesh):
    return jax.shard_map(
        body,
        mesh=mesh,
        in_specs=(
            P("sample", None, "depth", None, None),
            P("sample", None, "depth", None, None),
            P("sample", None, None, "depth", None),
            P(),
            P(),
        ),
        out_specs=(P(), P(), P("sample", None, "depth", None, None)),
        check_vma=False,
    )
```
